32 devices in a mesh: section: 4 (over y, x), expert: 8 (over z, core).
Axes of the slice: x: 2, y: 2, z: 4, core: 2. Of those that a mesh axis runs over, the one named last changes fastest.
Arguments:
- layer_inputs: bfloat16 [4, 16, 64, 4096], P('section', None, 'expert'), may hold values from -6 to 6
- expert_ids: int32 [4, 16, 64, 2], P('section', None, 'expert'), may hold values from 0 to 7, all different within a row; in each aligned block of 8 rows (0 to 7, 8 to 15, ..., all dimensions but the last counted through in order) at most 3 rows name the same one
- gates: bfloat16 [4, 16, 64, 2], P('section', None, 'expert'), may hold values from 0.099609375 to 0.59765625
- w_gate: bfloat16 [4, 4096, 4096], P('section', None, 'expert'), may hold values from -0.09375 to 0.09375
- w_up: bfloat16 [4, 4096, 4096], P('section', None, 'expert'), may hold values from -0.09375 to 0.09375
- w_down: bfloat16 [4, 4096, 4096], P('section', 'expert'), may hold values from -0.25 to 0.25
- out_grad: bfloat16 [16, 64, 4096], P(None, 'expert'), may hold values from -6 to 6
Outputs:
- section_grads: bfloat16 [4, 16, 64, 4096], P('section', None, 'expert')
The draws below stay inside these ranges and needn't reach their ends.
Inputs may be any that keep to these rules, and one draw needn't show every extreme that they name: `expert_ids`: within one micro-batch of one section, the 8 tokens of one expert index name each expert at most 3 times, and in some such groups one expert exactly 3 times; a token's 2 experts differ.
All inputs are finite; a program needn't handle non-finite values.
Results may differ from the reference program's by a relative error of at most 0.035.
Values may be sent and summed in bfloat16 or wider, within the bound.
No kernel may reach another device: no remote copies, remote signals or barrier semaphores. Data moves between devices by JAX's collectives and lax.ppermute only.
A program may use at most 64 MiB of HBM per device.

```python
import math
import jax
import jax.numpy as jnp
import numpy as np
from jax import lax

D = 4096
EXPERTS = 8
TOP = 2
FF_WIN = 512
TOK = 8
MB = 16
CAP = 3
SHARDS = 1
SECTION_TOKENS = 64
N_SECTION = 4
N_EXPERT = 8


def shard_levels(own_key, dims, shards, low, largest):
    def one(dim, parts):
        steps = jax.random.uniform(jax.random.fold_in(jax.random.fold_in(own_key, 6), dim), (parts,), jnp.float32, low / len(shards), largest / len(shards))
        return jnp.repeat(jnp.exp(steps), dims[dim] // parts).reshape((-1,) + (1,) * (len(dims) - dim - 1))

    loudness = one(*shards[0])
    for cut in shards[1:]:
        loudness = loudness * one(*cut)
    return loudness


def shared_out(stream_key, own, number, rows, number_of, top, bound, lean):
    order = jax.random.permutation(stream_key, number_of)
    crowded, common = load_shares(number_of, rows * top, bound, lean, True), load_shares(number_of, rows * top, bound, lean, False)
    places = jnp.arange(number_of)

    def named(tallies, turn):
        used = int((tallies > 0).sum())
        fixed = max(1, used // 4)
        shifted = fixed + (places - fixed + turn * (used - fixed)) % max(1, number_of - fixed)
        return jnp.zeros((number_of,), jnp.int32).at[order[jnp.where(places < fixed, places, shifted)]].set(jnp.asarray(tallies, jnp.int32))

    tallies = jnp.where(number % 4 == 0, named(crowded, number // 4), named(common, number - number // 4 - 1))
    mixed = jax.random.permutation(jax.random.fold_in(own, 3), number_of)
    donor, taker = mixed[0:number_of // 2 * 2:2], mixed[1:number_of // 2 * 2:2]
    room = jnp.minimum(tallies[donor] - 1, bound - tallies[taker]) // 2
    room = jnp.where((donor == order[0]) | (taker == order[0]) | (tallies[taker] == 0), 0, jnp.maximum(room, 0))
    shifted = jax.random.randint(jax.random.fold_in(own, 4), (number_of // 2,), 0, 1 << 20) % (room + 1)
    tallies = tallies.at[donor].add(-shifted).at[taker].add(shifted)
    labels = jnp.searchsorted(jnp.cumsum(tallies), jnp.arange(rows * top), side="right").astype(jnp.int32)
    table = labels.reshape(top, rows).T
    table = table[jax.random.permutation(jax.random.fold_in(own, 1), rows)]
    turn = jax.random.randint(jax.random.fold_in(own, 2), (rows, 1), 0, top)
    return jnp.take_along_axis(table, (jnp.arange(top)[None, :] + turn) % top, axis=1)


def load_shares(number_of, total, reach, lean, full):
    loads = [(1 << 20) // math.isqrt(grade ** lean) + 1 for grade in range(1, number_of + 1)]
    largest = reach if full else min(reach, max(-(-total // number_of), total * loads[0] // sum(loads)))
    least = 1 if total - largest >= number_of - 1 else 0
    holding, spare = [largest] + [least] * (number_of - 1), total - largest - least * (number_of - 1)
    while spare > 0:
        candidates = [i for i in range(1, number_of) if holding[i] < largest] or [i for i in range(1, number_of) if holding[i] < reach]
        pool, budget = sum([loads[i] for i in candidates]), spare
        for i in candidates:
            extra = min(reach - holding[i], max(1, budget * loads[i] // pool), spare)
            holding[i] = holding[i] + extra
            spare = spare - extra
    return np.array(holding)


def normal_values(own_key, shape, spread, reach, shards=(), held_as=jnp.bfloat16):
    gain = shard_levels(own_key, shape, shards, -0.22, 0.18) if shards else 1.0
    result = jax.random.normal(own_key, shape, jnp.float32) * spread * gain
    return jnp.minimum(jnp.maximum(result, -reach), reach).astype(held_as)


def setup_inputs(seed: int = 0) -> dict:
    splits = jax.random.split(jax.random.key(seed), 8)
    layer_inputs = normal_values(splits[0], (N_SECTION, MB, SECTION_TOKENS, D), 1.0, 6.0, ((0, 4), (2, 8)))
    expert_ids_keys = jax.random.split(jax.random.fold_in(splits[1], 1), N_SECTION * MB * SECTION_TOKENS // TOK)
    expert_ids_turns = jax.random.permutation(jax.random.fold_in(splits[1], 3), N_SECTION * MB * SECTION_TOKENS // TOK)
    expert_ids = jax.vmap(lambda own, number: shared_out(jax.random.fold_in(splits[1], 2), own, number, TOK, EXPERTS, TOP, CAP, 2))(expert_ids_keys, expert_ids_turns).reshape((N_SECTION, MB, SECTION_TOKENS, TOP))
    gates = jnp.clip(0.099609375 + 0.49804688 * jax.random.uniform(splits[2], (N_SECTION, MB, SECTION_TOKENS, TOP), jnp.float32) ** shard_levels(splits[2], (N_SECTION, MB, SECTION_TOKENS, TOP), ((0, 4), (2, 8)), -0.2, 0.2), 0.099609375, 0.59765625).astype(jnp.bfloat16)
    w_gate = normal_values(splits[3], (N_SECTION, D, EXPERTS * FF_WIN), D ** -0.5, 0.09375, ((0, 4), (2, 8)))
    w_up = normal_values(splits[4], (N_SECTION, D, EXPERTS * FF_WIN), D ** -0.5, 0.09375, ((0, 4), (2, 8)))
    w_down = normal_values(splits[5], (N_SECTION, EXPERTS * FF_WIN, D), FF_WIN ** -0.5, 0.25, ((0, 4), (1, 8)))
    out_grad = normal_values(splits[6], (MB, SECTION_TOKENS, D), 1.0, 6.0, ((1, 8),))
    return dict(layer_inputs=layer_inputs, expert_ids=expert_ids, gates=gates, w_gate=w_gate, w_up=w_up, w_down=w_down, out_grad=out_grad)


def selection(choices):
    experts = jnp.arange(EXPERTS, dtype=jnp.int32)
    onehot = (choices[..., None] == experts).astype(jnp.int32)
    leading = onehot.shape[:-3]
    flattened = onehot.reshape(leading + (TOK * TOP, EXPERTS))
    before = jnp.cumsum(flattened, axis=-2) - flattened
    slot_index = jnp.sum((before * flattened).reshape(onehot.shape), axis=-1)
    places = jnp.arange(CAP, dtype=jnp.int32)
    in_slot = (slot_index[..., None] == places).astype(jnp.int32)
    return onehot[..., None] * in_slot[..., None, :]


def reference(layer_inputs, expert_ids, gates, w_gate, w_up, w_down, out_grad):
    sources = N_EXPERT
    block_units = FF_WIN // SHARDS

    def one_section(incoming, section_data):
        inputs, choices, gate_values, gate_proj, up_proj, down_proj = section_data
        inputs = inputs.reshape(MB, sources, TOK, D).astype(jnp.float32)
        selected = selection(choices.reshape(MB, sources, TOK, TOP)).astype(jnp.float32)
        dispatch = jnp.sum(selected, axis=3)
        weights = gate_values.reshape(MB, sources, TOK, TOP).astype(jnp.float32)
        combine = jnp.sum(selected * weights[..., None, None], axis=3)
        gate_proj = gate_proj.astype(jnp.float32).reshape(D, EXPERTS, FF_WIN)
        up_proj = up_proj.astype(jnp.float32).reshape(D, EXPERTS, FF_WIN)
        down_proj = down_proj.astype(jnp.float32).reshape(EXPERTS, FF_WIN, D)
        token_rows = jnp.einsum('mstec,mstd->emscd', dispatch, inputs).reshape(EXPERTS, -1, D)
        pre_gate = jnp.einsum('erd,def->erf', token_rows, gate_proj)
        pre_up = jnp.einsum('erd,def->erf', token_rows, up_proj)
        sigmoid_gate = jax.nn.sigmoid(pre_gate)
        act = pre_gate * sigmoid_gate
        coef = pre_up * (sigmoid_gate * (1.0 + pre_gate * (1.0 - sigmoid_gate)))
        grad_out = incoming.astype(jnp.float32).reshape(MB, sources, TOK, D)
        grad_rows = jnp.einsum('mstec,mstd->emscd', dispatch, grad_out).reshape(EXPERTS, -1, D)
        down_grad = jnp.einsum('erd,efd->erf', grad_rows, down_proj)
        dgate = lax.optimization_barrier((down_grad * coef).astype(jnp.bfloat16)).astype(jnp.float32)
        dup = lax.optimization_barrier((down_grad * act).astype(jnp.bfloat16)).astype(jnp.float32)
        dgate = dgate.reshape(EXPERTS, -1, SHARDS, block_units)
        dup = dup.reshape(EXPERTS, -1, SHARDS, block_units)
        gate_blocks = gate_proj.reshape(D, EXPERTS, SHARDS, block_units)
        up_blocks = up_proj.reshape(D, EXPERTS, SHARDS, block_units)
        back = jnp.einsum('erkh,dekh->erkd', dgate, gate_blocks) + jnp.einsum('erkh,dekh->erkd', dup, up_blocks)
        back = lax.optimization_barrier(back.astype(jnp.bfloat16)).astype(jnp.float32)
        back = back.reshape(EXPERTS, MB, sources, CAP, SHARDS, D)
        mixed = jnp.einsum('mstec,emsckd->mstd', combine, back)
        grad_in = (grad_out + mixed).astype(jnp.bfloat16).reshape(MB, sources * TOK, D)
        return grad_in, grad_in

    section_data = (layer_inputs, expert_ids, gates, w_gate, w_up, w_down)
    final_grad, section_grads = lax.scan(one_section, out_grad, section_data, reverse=True)
    return section_grads
```

```python
import jax
import jax.numpy as jnp
from jax import lax
from jax.sharding import PartitionSpec as P

EXPERTS = 8
CAP = 3
CHUNK = 4


def passed_along(x, axis, by):
    length = lax.axis_size(axis)
    pairs = [(i, i + by) for i in range(length) if 0 <= i + by < length]
    return lax.ppermute(x, axis, pairs)


def selection(choices, capacity):
    token_count, top_count = (choices.shape[-2], choices.shape[-1])
    experts = jnp.arange(EXPERTS, dtype=jnp.int32)
    onehot = (choices[..., None] == experts).astype(jnp.int32)
    leading = onehot.shape[:-3]
    flattened = onehot.reshape(leading + (token_count * top_count, EXPERTS))
    before = jnp.cumsum(flattened, axis=-2) - flattened
    slot_index = jnp.sum((before * flattened).reshape(onehot.shape), axis=-1)
    places = jnp.arange(capacity, dtype=jnp.int32)
    in_slot = (slot_index[..., None] == places).astype(jnp.int32)
    return onehot[..., None] * in_slot[..., None, :]


def on_device(layer_inputs, expert_ids, gates, w_gate, w_up, w_down, out_grad):
    expert_count = lax.axis_size("expert")
    section_count = lax.axis_size("section")
    section_index = lax.axis_index("section")
    inputs = layer_inputs[0]
    gate_slice = w_gate[0]
    up_slice = w_up[0]
    down_slice = w_down[0]
    micro_count, token_count, model_width = inputs.shape
    hidden = gate_slice.shape[1]
    shards = expert_count // EXPERTS
    capacity = CAP
    slot_rows = expert_count * capacity
    chunk = CHUNK if micro_count % CHUNK == 0 else 1
    chunk_count = micro_count // chunk
    contract = (((1,), (1,)), ((), ()))
    selected = selection(expert_ids[0], capacity)
    dispatch = jnp.sum(selected, axis=2).astype(jnp.bfloat16)
    gate_values = gates[0].astype(jnp.float32)
    combine = jnp.sum(selected.astype(jnp.float32) * gate_values[..., None, None], axis=2).astype(
        jnp.bfloat16
    )

    def spread(rows):
        leading = rows.shape[:-3]
        rows = rows.astype(jnp.bfloat16)
        rows = jnp.broadcast_to(
            jnp.expand_dims(rows, -3), leading + (EXPERTS, shards, capacity, model_width)
        )
        return rows.reshape(leading + (expert_count, capacity, model_width))

    def backward_rows(grad_block, act, coef):
        down_grad = lax.dot_general(
            grad_block, down_slice, contract, preferred_element_type=jnp.float32
        )
        dgate = (down_grad * coef).astype(jnp.bfloat16)
        dup = (down_grad * act).astype(jnp.bfloat16)
        total = lax.dot_general(dgate, gate_slice, contract, preferred_element_type=jnp.float32)
        total = total + lax.dot_general(dup, up_slice, contract, preferred_element_type=jnp.float32)
        return total.astype(jnp.bfloat16)

    outgoing = spread(
        jnp.einsum("mtec,mtd->mecd", dispatch, inputs, preferred_element_type=jnp.float32)
    )
    received = lax.all_to_all(outgoing, "expert", split_axis=1, concat_axis=1, tiled=True)
    row_block = received.reshape(-1, model_width)
    pre_gate = jnp.dot(row_block, gate_slice, preferred_element_type=jnp.float32)
    pre_up = jnp.dot(row_block, up_slice, preferred_element_type=jnp.float32)
    sigmoid_gate = jax.nn.sigmoid(pre_gate)
    act = pre_gate * sigmoid_gate
    coef = pre_up * (sigmoid_gate * (1.0 + pre_gate * (1.0 - sigmoid_gate)))
    act_all = act.reshape(micro_count, slot_rows, hidden)
    coef_all = coef.reshape(micro_count, slot_rows, hidden)

    def tick(tick_index, state_pair):
        incoming, results = state_pair
        chunk_index = tick_index - (section_count - 1 - section_index)
        active = (chunk_index >= 0) & (chunk_index < chunk_count)
        start = jnp.clip(chunk_index, 0, chunk_count - 1) * chunk
        top_grad = lax.dynamic_slice_in_dim(out_grad, start, chunk, 0)
        grad_out = jnp.where(section_index == section_count - 1, top_grad, incoming)
        dispatch_chunk = lax.dynamic_slice_in_dim(dispatch, start, chunk, 0)
        combine_chunk = lax.dynamic_slice_in_dim(combine, start, chunk, 0)
        grad_rows = spread(
            jnp.einsum("mtec,mtd->mecd", dispatch_chunk, grad_out, preferred_element_type=jnp.float32)
        )
        arrived = lax.all_to_all(grad_rows, "expert", split_axis=1, concat_axis=1, tiled=True)
        act_chunk = lax.dynamic_slice_in_dim(act_all, start, chunk, 0).reshape(-1, hidden)
        coef_chunk = lax.dynamic_slice_in_dim(coef_all, start, chunk, 0).reshape(-1, hidden)
        back = backward_rows(arrived.reshape(-1, model_width), act_chunk, coef_chunk)
        returned = lax.all_to_all(
            back.reshape(chunk, expert_count, capacity, model_width),
            "expert",
            split_axis=1,
            concat_axis=1,
            tiled=True,
        )
        returned = returned.reshape(chunk, EXPERTS, shards, capacity, model_width)
        mixed = jnp.einsum(
            "mtec,mekcd->mtd", combine_chunk, returned, preferred_element_type=jnp.float32
        )
        grad_in = (grad_out.astype(jnp.float32) + mixed).astype(jnp.bfloat16)
        updated = lax.dynamic_update_slice_in_dim(results, grad_in, start, 0)
        results = jnp.where(active, updated, results)
        passed = passed_along(grad_in, "section", -1)
        return (passed, results)

    initial = (
        jnp.zeros((chunk, token_count, model_width), jnp.bfloat16),
        jnp.zeros((micro_count, token_count, model_width), jnp.bfloat16),
    )
    final_state = lax.fori_loop(0, chunk_count + section_count - 1, tick, initial)
    return final_state[1][None]


def solution(mesh):
    placed = (
        P("section", None, "expert", None),
        P("section", None, "expert", None),
        P("section", None, "expert", None),
        P("section", None, "expert"),
        P("section", None, "expert"),
        P("section", "expert", None),
        P(None, "expert", None),
    )
    return jax.shard_map(
        on_device,
        mesh=mesh,
        in_specs=placed,
        out_specs=P("section", None, "expert", None),
        check_vma=False,
    )
```

```python
import jax
import jax.numpy as jnp
from jax import lax
from jax.sharding import PartitionSpec as P

EXPERTS = 8
CAP = 3
CHUNK = 4


def passed_along(x, axis, by):
    length = lax.axis_size(axis)
    pairs = [(i, i + by) for i in range(length) if 0 <= i + by < length]
    return lax.ppermute(x, axis, pairs)


def selection(choices, capacity):
    token_count, top_count = (choices.shape[-2], choices.shape[-1])
    experts = jnp.arange(EXPERTS, dtype=jnp.int32)
    onehot = (choices[..., None] == experts).astype(jnp.int32)
    leading = onehot.shape[:-3]
    flattened = onehot.reshape(leading + (token_count * top_count, EXPERTS))
    before = jnp.cumsum(flattened, axis=-2) - flattened
    slot_index = jnp.sum((before * flattened).reshape(onehot.shape), axis=-1)
    places = jnp.arange(capacity, dtype=jnp.int32)
    in_slot = (slot_index[..., None] == places).astype(jnp.int32)
    return onehot[..., None] * in_slot[..., None, :]


def on_device(layer_inputs, expert_ids, gates, w_gate, w_up, w_down, out_grad):
    expert_count = lax.axis_size("expert")
    section_count = lax.axis_size("section")
    section_index = lax.axis_index("section")
    inputs = layer_inputs[0]
    gate_slice = w_gate[0]
    up_slice = w_up[0]
    down_t = w_down[0].T
    micro_count, token_count, model_width = inputs.shape
    hidden = gate_slice.shape[1]
    shards = expert_count // EXPERTS
    capacity = CAP
    slot_rows = expert_count * capacity
    chunk = CHUNK if micro_count % CHUNK == 0 else 1
    chunk_count = micro_count // chunk
    contract = (((1,), (1,)), ((), ()))
    selected = selection(expert_ids[0], capacity)
    dispatch = jnp.sum(selected, axis=2).astype(jnp.bfloat16)
    gate_values = gates[0].astype(jnp.float32)
    combine = jnp.sum(selected.astype(jnp.float32) * gate_values[..., None, None], axis=2).astype(
        jnp.bfloat16
    )

    def spread(rows):
        trailing = rows.shape[1:]
        rows = rows.astype(jnp.bfloat16)
        rows = jnp.broadcast_to(rows[:, None], (EXPERTS, shards) + trailing)
        return rows.reshape((expert_count,) + trailing)

    def backward_rows(grad_block, act, coef):
        down_grad = jnp.dot(grad_block, down_t, preferred_element_type=jnp.float32)
        dgate = (down_grad * coef).astype(jnp.bfloat16)
        dup = (down_grad * act).astype(jnp.bfloat16)
        total = lax.dot_general(dgate, gate_slice, contract, preferred_element_type=jnp.float32)
        total = total + lax.dot_general(dup, up_slice, contract, preferred_element_type=jnp.float32)
        return total.astype(jnp.bfloat16)

    def forward_chunk(first):
        inputs_chunk = lax.slice_in_dim(inputs, first, first + chunk, axis=0)
        dispatch_part = lax.slice_in_dim(dispatch, first, first + chunk, axis=0)
        outgoing = spread(
            jnp.einsum("mtec,mtd->emcd", dispatch_part, inputs_chunk, preferred_element_type=jnp.float32)
        )
        received = lax.all_to_all(outgoing, "expert", split_axis=0, concat_axis=0, tiled=True)
        row_block = received.reshape(-1, model_width)
        pre_gate = jnp.dot(row_block, gate_slice, preferred_element_type=jnp.float32)
        pre_up = jnp.dot(row_block, up_slice, preferred_element_type=jnp.float32)
        sigmoid_gate = jax.nn.sigmoid(pre_gate)
        act = pre_gate * sigmoid_gate
        coef = pre_up * (sigmoid_gate * (1.0 + pre_gate * (1.0 - sigmoid_gate)))
        return (
            act.reshape(expert_count, chunk, capacity, hidden),
            coef.reshape(expert_count, chunk, capacity, hidden),
        )

    def tick(tick_index, state_pair):
        incoming, results, act_all, coef_all = state_pair
        if tick_index < chunk_count:
            act_new, coef_new = forward_chunk(tick_index * chunk)
            act_all = lax.dynamic_update_slice_in_dim(act_all, act_new, tick_index * chunk, 1)
            coef_all = lax.dynamic_update_slice_in_dim(coef_all, coef_new, tick_index * chunk, 1)
        chunk_index = tick_index - (section_count - 1 - section_index)
        active = (chunk_index >= 0) & (chunk_index < chunk_count)
        start = jnp.clip(chunk_index, 0, chunk_count - 1) * chunk
        top_grad = lax.dynamic_slice_in_dim(out_grad, start, chunk, 0)
        grad_out = jnp.where(section_index == section_count - 1, top_grad, incoming)
        dispatch_chunk = lax.dynamic_slice_in_dim(dispatch, start, chunk, 0)
        combine_chunk = lax.dynamic_slice_in_dim(combine, start, chunk, 0)
        grad_rows = spread(
            jnp.einsum("mtec,mtd->emcd", dispatch_chunk, grad_out, preferred_element_type=jnp.float32)
        )
        arrived = lax.all_to_all(grad_rows, "expert", split_axis=0, concat_axis=0, tiled=True)
        act_chunk = lax.dynamic_slice_in_dim(act_all, start, chunk, 1).reshape(-1, hidden)
        coef_chunk = lax.dynamic_slice_in_dim(coef_all, start, chunk, 1).reshape(-1, hidden)
        back = backward_rows(arrived.reshape(-1, model_width), act_chunk, coef_chunk)
        returned = lax.all_to_all(
            back.reshape(expert_count, chunk, capacity, model_width),
            "expert",
            split_axis=0,
            concat_axis=0,
            tiled=True,
        )
        returned = returned.reshape(EXPERTS, shards, chunk, capacity, model_width)
        mixed = jnp.einsum(
            "mtec,ekmcd->mtd", combine_chunk, returned, preferred_element_type=jnp.float32
        )
        grad_in = (grad_out.astype(jnp.float32) + mixed).astype(jnp.bfloat16)
        slot = (jnp.clip(chunk_index, -1, chunk_count) + 1) * chunk
        results = lax.dynamic_update_slice_in_dim(results, grad_in, slot, 0)
        passed = passed_along(grad_in, "section", -1)
        return (passed, results, act_all, coef_all)

    initial = (
        jnp.zeros((chunk, token_count, model_width), jnp.bfloat16),
        jnp.zeros((micro_count + 2 * chunk, token_count, model_width), jnp.bfloat16),
        jnp.zeros((expert_count, micro_count, capacity, hidden), jnp.float32),
        jnp.zeros((expert_count, micro_count, capacity, hidden), jnp.float32),
    )
    final_state = initial
    for tick_index in range(chunk_count + section_count - 1):
        final_state = tick(tick_index, final_state)
    return final_state[1][chunk : chunk + micro_count][None]


def solution(mesh):
    placed = (
        P("section", None, "expert", None),
        P("section", None, "expert", None),
        P("section", None, "expert", None),
        P("section", None, "expert"),
        P("section", None, "expert"),
        P("section", "expert", None),
        P(None, "expert", None),
    )
    return jax.shard_map(
        on_device,
        mesh=mesh,
        in_specs=placed,
        out_specs=P("section", None, "expert", None),
        check_vma=False,
    )
```

```python
import jax
import jax.numpy as jnp
from jax import lax
from jax.sharding import PartitionSpec as P

EXPERTS = 8
CAP = 3
CHUNK = 4


def passed_along(x, axis, by):
    length = lax.axis_size(axis)
    pairs = [(i, i + by) for i in range(length) if 0 <= i + by < length]
    return lax.ppermute(x, axis, pairs)


def selection(choices, capacity):
    token_count, top_count = (choices.shape[-2], choices.shape[-1])
    experts = jnp.arange(EXPERTS, dtype=jnp.int32)
    onehot = (choices[..., None] == experts).astype(jnp.int32)
    leading = onehot.shape[:-3]
    flattened = onehot.reshape(leading + (token_count * top_count, EXPERTS))
    before = jnp.cumsum(flattened, axis=-2) - flattened
    slot_index = jnp.sum((before * flattened).reshape(onehot.shape), axis=-1)
    places = jnp.arange(capacity, dtype=jnp.int32)
    in_slot = (slot_index[..., None] == places).astype(jnp.int32)
    return onehot[..., None] * in_slot[..., None, :]


def on_device(layer_inputs, expert_ids, gates, w_gate, w_up, w_down, out_grad):
    expert_count = lax.axis_size("expert")
    section_count = lax.axis_size("section")
    section_index = lax.axis_index("section")
    inputs = layer_inputs[0]
    gate_slice = w_gate[0]
    up_slice = w_up[0]
    down_t = w_down[0].T
    micro_count, token_count, model_width = inputs.shape
    hidden = gate_slice.shape[1]
    shards = expert_count // EXPERTS
    capacity = CAP
    slot_rows = expert_count * capacity
    chunk = CHUNK if micro_count % CHUNK == 0 else 1
    chunk_count = micro_count // chunk
    contract = (((1,), (1,)), ((), ()))
    selected = selection(expert_ids[0], capacity)
    dispatch = jnp.sum(selected, axis=2).astype(jnp.bfloat16)
    gate_values = gates[0].astype(jnp.float32)
    combine = jnp.sum(selected.astype(jnp.float32) * gate_values[..., None, None], axis=2).astype(
        jnp.bfloat16
    )

    def spread(rows):
        trailing = rows.shape[1:]
        rows = rows.astype(jnp.bfloat16)
        rows = jnp.broadcast_to(rows[:, None], (EXPERTS, shards) + trailing)
        return rows.reshape((expert_count,) + trailing)

    def backward_rows(grad_block, act, coef):
        down_grad = jnp.dot(grad_block, down_t, preferred_element_type=jnp.float32)
        dgate = (down_grad * coef).astype(jnp.bfloat16)
        dup = (down_grad * act).astype(jnp.bfloat16)
        total = lax.dot_general(dgate, gate_slice, contract, preferred_element_type=jnp.float32)
        total = total + lax.dot_general(dup, up_slice, contract, preferred_element_type=jnp.float32)
        return total.astype(jnp.bfloat16)

    def forward_chunk(first):
        inputs_chunk = lax.slice_in_dim(inputs, first, first + chunk, axis=0)
        dispatch_part = lax.slice_in_dim(dispatch, first, first + chunk, axis=0)
        outgoing = spread(
            jnp.einsum("mtec,mtd->ecmd", dispatch_part, inputs_chunk, preferred_element_type=jnp.float32)
        )
        received = lax.all_to_all(outgoing, "expert", split_axis=0, concat_axis=0, tiled=True)
        row_block = received.reshape(-1, model_width)
        pre_gate = jnp.dot(row_block, gate_slice, preferred_element_type=jnp.float32)
        pre_up = jnp.dot(row_block, up_slice, preferred_element_type=jnp.float32)
        sigmoid_gate = jax.nn.sigmoid(pre_gate)
        act = pre_gate * sigmoid_gate
        coef = pre_up * (sigmoid_gate * (1.0 + pre_gate * (1.0 - sigmoid_gate)))
        return act, coef

    def tick(tick_index, state_pair):
        incoming, results, act_all, coef_all = state_pair
        if tick_index < chunk_count:
            act_new, coef_new = forward_chunk(tick_index * chunk)
            act_all = act_all.at[tick_index].set(act_new)
            coef_all = coef_all.at[tick_index].set(coef_new)
        chunk_index = tick_index - (section_count - 1 - section_index)
        active = (chunk_index >= 0) & (chunk_index < chunk_count)
        start = jnp.clip(chunk_index, 0, chunk_count - 1) * chunk
        top_grad = lax.dynamic_slice_in_dim(out_grad, start, chunk, 0)
        grad_out = jnp.where(section_index == section_count - 1, top_grad, incoming)
        dispatch_chunk = lax.dynamic_slice_in_dim(dispatch, start, chunk, 0)
        combine_chunk = lax.dynamic_slice_in_dim(combine, start, chunk, 0)
        grad_rows = spread(
            jnp.einsum("mtec,mtd->ecmd", dispatch_chunk, grad_out, preferred_element_type=jnp.float32)
        )
        arrived = lax.all_to_all(grad_rows, "expert", split_axis=0, concat_axis=0, tiled=True)
        act_chunk = lax.dynamic_index_in_dim(act_all, start // chunk, 0, keepdims=False)
        coef_chunk = lax.dynamic_index_in_dim(coef_all, start // chunk, 0, keepdims=False)
        back = backward_rows(arrived.reshape(-1, model_width), act_chunk, coef_chunk)
        returned = lax.all_to_all(
            back.reshape(expert_count, capacity, chunk, model_width),
            "expert",
            split_axis=0,
            concat_axis=0,
            tiled=True,
        )
        returned = returned.reshape(EXPERTS, shards, capacity, chunk, model_width)
        mixed = jnp.einsum(
            "mtec,ekcmd->mtd", combine_chunk, returned, preferred_element_type=jnp.float32
        )
        grad_in = (grad_out.astype(jnp.float32) + mixed).astype(jnp.bfloat16)
        slot = (jnp.clip(chunk_index, -1, chunk_count) + 1) * chunk
        results = lax.dynamic_update_slice_in_dim(results, grad_in, slot, 0)
        passed = passed_along(grad_in, "section", -1)
        return (passed, results, act_all, coef_all)

    initial = (
        jnp.zeros((chunk, token_count, model_width), jnp.bfloat16),
        jnp.zeros((micro_count + 2 * chunk, token_count, model_width), jnp.bfloat16),
        jnp.zeros((chunk_count, expert_count * chunk * capacity, hidden), jnp.float32),
        jnp.zeros((chunk_count, expert_count * chunk * capacity, hidden), jnp.float32),
    )
    final_state = initial
    for tick_index in range(chunk_count + section_count - 1):
        final_state = tick(tick_index, final_state)
    return final_state[1][chunk : chunk + micro_count][None]


def solution(mesh):
    placed = (
        P("section", None, "expert", None),
        P("section", None, "expert", None),
        P("section", None, "expert", None),
        P("section", None, "expert"),
        P("section", None, "expert"),
        P("section", "expert", None),
        P(None, "expert", None),
    )
    return jax.shard_map(
        on_device,
        mesh=mesh,
        in_specs=placed,
        out_specs=P("section", None, "expert", None),
        check_vma=False,
    )
```

```python
import jax
import jax.numpy as jnp
from jax import lax
from jax.sharding import PartitionSpec as P

EXPERTS = 8
CAP = 3
CHUNK = 4


def passed_along(x, axis, by):
    length = lax.axis_size(axis)
    pairs = [(i, i + by) for i in range(length) if 0 <= i + by < length]
    return lax.ppermute(x, axis, pairs)


def selection(choices, capacity):
    token_count, top_count = (choices.shape[-2], choices.shape[-1])
    experts = jnp.arange(EXPERTS, dtype=jnp.int32)
    onehot = (choices[..., None] == experts).astype(jnp.int32)
    leading = onehot.shape[:-3]
    flattened = onehot.reshape(leading + (token_count * top_count, EXPERTS))
    before = jnp.cumsum(flattened, axis=-2) - flattened
    slot_index = jnp.sum((before * flattened).reshape(onehot.shape), axis=-1)
    places = jnp.arange(capacity, dtype=jnp.int32)
    in_slot = (slot_index[..., None] == places).astype(jnp.int32)
    return onehot[..., None] * in_slot[..., None, :]


def on_device(layer_inputs, expert_ids, gates, w_gate, w_up, w_down, out_grad):
    expert_count = lax.axis_size("expert")
    section_count = lax.axis_size("section")
    section_index = lax.axis_index("section")
    inputs = layer_inputs[0]
    gate_slice = w_gate[0]
    up_slice = w_up[0]
    down_t = w_down[0].T
    micro_count, token_count, model_width = inputs.shape
    hidden = gate_slice.shape[1]
    shards = expert_count // EXPERTS
    capacity = CAP
    slot_rows = expert_count * capacity
    chunk = CHUNK if micro_count % CHUNK == 0 else 1
    chunk_count = micro_count // chunk
    contract = (((1,), (1,)), ((), ()))
    selected = selection(expert_ids[0], capacity)
    dispatch = jnp.sum(selected, axis=2).astype(jnp.bfloat16)
    gate_values = gates[0].astype(jnp.float32)
    combine = jnp.sum(selected.astype(jnp.float32) * gate_values[..., None, None], axis=2).astype(
        jnp.bfloat16
    )

    def spread(rows):
        trailing = rows.shape[1:]
        rows = rows.astype(jnp.bfloat16)
        rows = jnp.broadcast_to(rows[:, None], (EXPERTS, shards) + trailing)
        return rows.reshape((expert_count,) + trailing)

    def backward_rows(grad_block, act, coef):
        down_grad = jnp.dot(grad_block, down_t, preferred_element_type=jnp.float32)
        dgate = (down_grad * coef).astype(jnp.bfloat16)
        dup = (down_grad * act).astype(jnp.bfloat16)
        total = lax.dot_general(dgate, gate_slice, contract, preferred_element_type=jnp.float32)
        total = total + lax.dot_general(dup, up_slice, contract, preferred_element_type=jnp.float32)
        return total.astype(jnp.bfloat16)

    def forward_chunk(first):
        inputs_chunk = lax.slice_in_dim(inputs, first, first + chunk, axis=0)
        dispatch_part = lax.slice_in_dim(dispatch, first, first + chunk, axis=0)
        outgoing = spread(
            jnp.einsum("mtec,mtd->ecmd", dispatch_part, inputs_chunk, preferred_element_type=jnp.float32)
        )
        received = lax.all_to_all(outgoing, "expert", split_axis=0, concat_axis=0, tiled=True)
        row_block = received.reshape(-1, model_width)
        pre_gate = jnp.dot(row_block, gate_slice, preferred_element_type=jnp.float32)
        pre_up = jnp.dot(row_block, up_slice, preferred_element_type=jnp.float32)
        sigmoid_gate = jax.nn.sigmoid(pre_gate)
        act = pre_gate * sigmoid_gate
        coef = pre_up * (sigmoid_gate * (1.0 + pre_gate * (1.0 - sigmoid_gate)))
        return act, coef

    def tick(tick_index, state_pair):
        incoming, results, act_all, coef_all = state_pair
        if isinstance(tick_index, int):
            act_new, coef_new = forward_chunk(tick_index * chunk)
            act_all = act_all.at[tick_index].set(act_new)
            coef_all = coef_all.at[tick_index].set(coef_new)
        chunk_index = tick_index - (section_count - 1 - section_index)
        active = (chunk_index >= 0) & (chunk_index < chunk_count)
        start = jnp.clip(chunk_index, 0, chunk_count - 1) * chunk
        top_grad = lax.dynamic_slice_in_dim(out_grad, start, chunk, 0)
        grad_out = jnp.where(section_index == section_count - 1, top_grad, incoming)
        dispatch_chunk = lax.dynamic_slice_in_dim(dispatch, start, chunk, 0)
        combine_chunk = lax.dynamic_slice_in_dim(combine, start, chunk, 0)
        grad_rows = spread(
            jnp.einsum("mtec,mtd->ecmd", dispatch_chunk, grad_out, preferred_element_type=jnp.float32)
        )
        arrived = lax.all_to_all(grad_rows, "expert", split_axis=0, concat_axis=0, tiled=True)
        act_chunk = lax.dynamic_index_in_dim(act_all, start // chunk, 0, keepdims=False)
        coef_chunk = lax.dynamic_index_in_dim(coef_all, start // chunk, 0, keepdims=False)
        back = backward_rows(arrived.reshape(-1, model_width), act_chunk, coef_chunk)
        returned = lax.all_to_all(
            back.reshape(expert_count, capacity, chunk, model_width),
            "expert",
            split_axis=0,
            concat_axis=0,
            tiled=True,
        )
        returned = returned.reshape(EXPERTS, shards, capacity, chunk, model_width)
        mixed = jnp.einsum(
            "mtec,ekcmd->mtd", combine_chunk, returned, preferred_element_type=jnp.float32
        )
        grad_in = (grad_out.astype(jnp.float32) + mixed).astype(jnp.bfloat16)
        slot = (jnp.clip(chunk_index, -1, chunk_count) + 1) * chunk
        results = lax.dynamic_update_slice_in_dim(results, grad_in, slot, 0)
        passed = passed_along(grad_in, "section", -1)
        return (passed, results, act_all, coef_all)

    initial = (
        jnp.zeros((chunk, token_count, model_width), jnp.bfloat16),
        jnp.zeros((micro_count + 2 * chunk, token_count, model_width), jnp.bfloat16),
        jnp.zeros((chunk_count, expert_count * chunk * capacity, hidden), jnp.float32),
        jnp.zeros((chunk_count, expert_count * chunk * capacity, hidden), jnp.float32),
    )
    final_state = initial
    for tick_index in range(chunk_count):
        final_state = tick(tick_index, final_state)
    final_state = lax.fori_loop(
        chunk_count, chunk_count + section_count - 1, tick, final_state
    )
    return final_state[1][chunk : chunk + micro_count][None]


def solution(mesh):
    placed = (
        P("section", None, "expert", None),
        P("section", None, "expert", None),
        P("section", None, "expert", None),
        P("section", None, "expert"),
        P("section", None, "expert"),
        P("section", "expert", None),
        P(None, "expert", None),
    )
    return jax.shard_map(
        on_device,
        mesh=mesh,
        in_specs=placed,
        out_specs=P("section", None, "expert", None),
        check_vma=False,
    )
```

```python
import jax
import jax.numpy as jnp
from jax import lax
from jax.sharding import PartitionSpec as P

EXPERTS = 8
CAP = 3
CHUNK = 4


def passed_along(x, axis, by):
    length = lax.axis_size(axis)
    pairs = [(i, i + by) for i in range(length) if 0 <= i + by < length]
    return lax.ppermute(x, axis, pairs)


def selection(choices, capacity):
    token_count, top_count = (choices.shape[-2], choices.shape[-1])
    experts = jnp.arange(EXPERTS, dtype=jnp.int32)
    onehot = (choices[..., None] == experts).astype(jnp.int32)
    leading = onehot.shape[:-3]
    flattened = onehot.reshape(leading + (token_count * top_count, EXPERTS))
    before = jnp.cumsum(flattened, axis=-2) - flattened
    slot_index = jnp.sum((before * flattened).reshape(onehot.shape), axis=-1)
    places = jnp.arange(capacity, dtype=jnp.int32)
    in_slot = (slot_index[..., None] == places).astype(jnp.int32)
    return onehot[..., None] * in_slot[..., None, :]


def on_device(layer_inputs, expert_ids, gates, w_gate, w_up, w_down, out_grad):
    expert_count = lax.axis_size("expert")
    section_count = lax.axis_size("section")
    section_index = lax.axis_index("section")
    inputs = layer_inputs[0]
    gate_slice = w_gate[0]
    up_slice = w_up[0]
    down_t = w_down[0].T
    micro_count, token_count, model_width = inputs.shape
    hidden = gate_slice.shape[1]
    shards = expert_count // EXPERTS
    capacity = CAP
    slot_rows = expert_count * capacity
    chunk = CHUNK if micro_count % CHUNK == 0 else 1
    chunk_count = micro_count // chunk
    contract = (((1,), (1,)), ((), ()))
    selected = selection(expert_ids[0], capacity)
    dispatch = jnp.sum(selected, axis=2).astype(jnp.bfloat16)
    gate_values = gates[0].astype(jnp.float32)
    combine = jnp.sum(selected.astype(jnp.float32) * gate_values[..., None, None], axis=2).astype(
        jnp.bfloat16
    )

    def spread(rows):
        trailing = rows.shape[1:]
        rows = rows.astype(jnp.bfloat16)
        rows = jnp.broadcast_to(rows[:, None], (EXPERTS, shards) + trailing)
        return rows.reshape((expert_count,) + trailing)

    def backward_rows(grad_block, act, coef):
        down_grad = jnp.dot(grad_block, down_t, preferred_element_type=jnp.float32)
        dgate = (down_grad * coef).astype(jnp.bfloat16)
        dup = (down_grad * act).astype(jnp.bfloat16)
        total = lax.dot_general(dgate, gate_slice, contract, preferred_element_type=jnp.float32)
        total = total + lax.dot_general(dup, up_slice, contract, preferred_element_type=jnp.float32)
        return total.astype(jnp.bfloat16)

    def forward_chunk(first):
        inputs_chunk = lax.slice_in_dim(inputs, first, first + chunk, axis=0)
        dispatch_part = lax.slice_in_dim(dispatch, first, first + chunk, axis=0)
        outgoing = spread(
            jnp.einsum("mtec,mtd->ecmd", dispatch_part, inputs_chunk, preferred_element_type=jnp.float32)
        )
        received = lax.all_to_all(outgoing, "expert", split_axis=0, concat_axis=0, tiled=True)
        row_block = received.reshape(-1, model_width)
        pre_gate = jnp.dot(row_block, gate_slice, preferred_element_type=jnp.float32)
        pre_up = jnp.dot(row_block, up_slice, preferred_element_type=jnp.float32)
        sigmoid_gate = jax.nn.sigmoid(pre_gate)
        act = pre_gate * sigmoid_gate
        coef = pre_up * (sigmoid_gate * (1.0 + pre_gate * (1.0 - sigmoid_gate)))
        return act, coef

    def tick(tick_index, state_pair):
        incoming, results, act_all, coef_all = state_pair
        if tick_index < chunk_count:
            act_new, coef_new = forward_chunk(tick_index * chunk)
            act_all = act_all.at[tick_index].set(act_new)
            coef_all = coef_all.at[tick_index].set(coef_new)
        chunk_index = tick_index - (section_count - 1 - section_index)
        active = (chunk_index >= 0) & (chunk_index < chunk_count)
        start = jnp.clip(chunk_index, 0, chunk_count - 1) * chunk
        top_grad = lax.dynamic_slice_in_dim(out_grad, start, chunk, 0)
        grad_out = jnp.where(section_index == section_count - 1, top_grad, incoming)
        dispatch_chunk = lax.dynamic_slice_in_dim(dispatch, start, chunk, 0)
        combine_chunk = lax.dynamic_slice_in_dim(combine, start, chunk, 0)
        grad_rows = spread(
            jnp.einsum("mtec,mtd->ecmd", dispatch_chunk, grad_out, preferred_element_type=jnp.float32)
        )
        arrived = lax.all_to_all(grad_rows, "expert", split_axis=0, concat_axis=0, tiled=True)
        act_chunk = lax.dynamic_index_in_dim(act_all, start // chunk, 0, keepdims=False)
        coef_chunk = lax.dynamic_index_in_dim(coef_all, start // chunk, 0, keepdims=False)
        back = backward_rows(arrived.reshape(-1, model_width), act_chunk, coef_chunk)
        returned = lax.all_to_all(
            back.reshape(expert_count, capacity, chunk, model_width),
            "expert",
            split_axis=0,
            concat_axis=0,
            tiled=True,
        )
        returned = returned.reshape(EXPERTS, shards, capacity, chunk, model_width)
        mixed = jnp.einsum(
            "mtec,ekcmd->mtd", combine_chunk, returned, preferred_element_type=jnp.float32
        )
        grad_in = (grad_out.astype(jnp.float32) + mixed).astype(jnp.bfloat16)
        slot = (jnp.clip(chunk_index, -1, chunk_count) + 1) * chunk
        passed = passed_along(grad_in, "section", -1)
        results = lax.dynamic_update_slice_in_dim(results, lax.optimization_barrier(grad_in), slot, 0)
        return (passed, results, act_all, coef_all)

    initial = (
        jnp.zeros((chunk, token_count, model_width), jnp.bfloat16),
        jnp.zeros((micro_count + 2 * chunk, token_count, model_width), jnp.bfloat16),
        jnp.zeros((chunk_count, expert_count * chunk * capacity, hidden), jnp.float32),
        jnp.zeros((chunk_count, expert_count * chunk * capacity, hidden), jnp.float32),
    )
    final_state = initial
    for tick_index in range(chunk_count + section_count - 1):
        final_state = tick(tick_index, final_state)
    return final_state[1][chunk : chunk + micro_count][None]


def solution(mesh):
    placed = (
        P("section", None, "expert", None),
        P("section", None, "expert", None),
        P("section", None, "expert", None),
        P("section", None, "expert"),
        P("section", None, "expert"),
        P("section", "expert", None),
        P(None, "expert", None),
    )
    return jax.shard_map(
        on_device,
        mesh=mesh,
        in_specs=placed,
        out_specs=P("section", None, "expert", None),
        check_vma=False,
    )
```

```python
import jax
import jax.numpy as jnp
from jax import lax
from jax.sharding import PartitionSpec as P

EXPERTS = 8
CAP = 3
CHUNK = 4


def passed_along(x, axis, by):
    length = lax.axis_size(axis)
    pairs = [(i, i + by) for i in range(length) if 0 <= i + by < length]
    return lax.ppermute(x, axis, pairs)


def exchange(blocks, axis, direction):
    count = blocks.shape[0]
    moved = [blocks[0]]
    for shift in range(1, count):
        pairs = [(i, (i + direction * shift) % count) for i in range(count)]
        moved.append(lax.ppermute(blocks[shift], axis, pairs))
    return jnp.stack(moved)


def selection(choices, capacity):
    token_count, top_count = (choices.shape[-2], choices.shape[-1])
    experts = jnp.arange(EXPERTS, dtype=jnp.int32)
    onehot = (choices[..., None] == experts).astype(jnp.int32)
    leading = onehot.shape[:-3]
    flattened = onehot.reshape(leading + (token_count * top_count, EXPERTS))
    before = jnp.cumsum(flattened, axis=-2) - flattened
    slot_index = jnp.sum((before * flattened).reshape(onehot.shape), axis=-1)
    places = jnp.arange(capacity, dtype=jnp.int32)
    in_slot = (slot_index[..., None] == places).astype(jnp.int32)
    return onehot[..., None] * in_slot[..., None, :]


def on_device(layer_inputs, expert_ids, gates, w_gate, w_up, w_down, out_grad):
    expert_count = lax.axis_size("expert")
    section_count = lax.axis_size("section")
    section_index = lax.axis_index("section")
    inputs = layer_inputs[0]
    gate_slice = w_gate[0]
    up_slice = w_up[0]
    down_t = w_down[0].T
    micro_count, token_count, model_width = inputs.shape
    hidden = gate_slice.shape[1]
    shards = expert_count // EXPERTS
    capacity = CAP
    slot_rows = expert_count * capacity
    chunk = CHUNK if micro_count % CHUNK == 0 else 1
    chunk_count = micro_count // chunk
    contract = (((1,), (1,)), ((), ()))
    selected = selection(expert_ids[0], capacity)
    dispatch = jnp.sum(selected, axis=2).astype(jnp.bfloat16)
    gate_values = gates[0].astype(jnp.float32)
    combine = jnp.sum(selected.astype(jnp.float32) * gate_values[..., None, None], axis=2).astype(
        jnp.bfloat16
    )

    def spread(rows):
        trailing = rows.shape[1:]
        rows = rows.astype(jnp.bfloat16)
        rows = jnp.broadcast_to(rows[:, None], (EXPERTS, shards) + trailing)
        return rows.reshape((expert_count,) + trailing)

    def backward_rows(grad_block, act, coef):
        down_grad = jnp.dot(grad_block, down_t, preferred_element_type=jnp.float32)
        dgate = (down_grad * coef).astype(jnp.bfloat16)
        dup = (down_grad * act).astype(jnp.bfloat16)
        total = lax.dot_general(dgate, gate_slice, contract, preferred_element_type=jnp.float32)
        total = total + lax.dot_general(dup, up_slice, contract, preferred_element_type=jnp.float32)
        return total.astype(jnp.bfloat16)

    def forward_chunk(first):
        inputs_chunk = lax.slice_in_dim(inputs, first, first + chunk, axis=0)
        dispatch_part = lax.slice_in_dim(dispatch, first, first + chunk, axis=0)
        outgoing = spread(
            jnp.einsum("mtec,mtd->ecmd", dispatch_part, inputs_chunk, preferred_element_type=jnp.float32)
        )
        if first == 0:
            index = lax.axis_index("expert")
            places = jnp.arange(expert_count)
            rotated = jnp.take(outgoing, (index + places) % expert_count, axis=0)
            received = exchange(rotated, "expert", 1)
            received = jnp.take(received, (index - places) % expert_count, axis=0)
        else:
            received = lax.all_to_all(outgoing, "expert", split_axis=0, concat_axis=0, tiled=True)
        row_block = received.reshape(-1, model_width)
        pre_gate = jnp.dot(row_block, gate_slice, preferred_element_type=jnp.float32)
        pre_up = jnp.dot(row_block, up_slice, preferred_element_type=jnp.float32)
        sigmoid_gate = jax.nn.sigmoid(pre_gate)
        act = pre_gate * sigmoid_gate
        coef = pre_up * (sigmoid_gate * (1.0 + pre_gate * (1.0 - sigmoid_gate)))
        return act, coef

    def tick(tick_index, state_pair):
        incoming, results, act_all, coef_all = state_pair
        if tick_index < chunk_count:
            act_new, coef_new = forward_chunk(tick_index * chunk)
            act_all = act_all.at[tick_index].set(act_new)
            coef_all = coef_all.at[tick_index].set(coef_new)
        chunk_index = tick_index - (section_count - 1 - section_index)
        active = (chunk_index >= 0) & (chunk_index < chunk_count)
        start = jnp.clip(chunk_index, 0, chunk_count - 1) * chunk
        top_grad = lax.dynamic_slice_in_dim(out_grad, start, chunk, 0)
        grad_out = jnp.where(section_index == section_count - 1, top_grad, incoming)
        dispatch_chunk = lax.dynamic_slice_in_dim(dispatch, start, chunk, 0)
        combine_chunk = lax.dynamic_slice_in_dim(combine, start, chunk, 0)
        grad_rows = spread(
            jnp.einsum("mtec,mtd->ecmd", dispatch_chunk, grad_out, preferred_element_type=jnp.float32)
        )
        arrived = lax.all_to_all(grad_rows, "expert", split_axis=0, concat_axis=0, tiled=True)
        act_chunk = lax.dynamic_index_in_dim(act_all, start // chunk, 0, keepdims=False)
        coef_chunk = lax.dynamic_index_in_dim(coef_all, start // chunk, 0, keepdims=False)
        back = backward_rows(arrived.reshape(-1, model_width), act_chunk, coef_chunk)
        returned = lax.all_to_all(
            back.reshape(expert_count, capacity, chunk, model_width),
            "expert",
            split_axis=0,
            concat_axis=0,
            tiled=True,
        )
        returned = returned.reshape(EXPERTS, shards, capacity, chunk, model_width)
        mixed = jnp.einsum(
            "mtec,ekcmd->mtd", combine_chunk, returned, preferred_element_type=jnp.float32
        )
        grad_in = (grad_out.astype(jnp.float32) + mixed).astype(jnp.bfloat16)
        slot = (jnp.clip(chunk_index, -1, chunk_count) + 1) * chunk
        passed = passed_along(grad_in, "section", -1)
        results = lax.dynamic_update_slice_in_dim(results, lax.optimization_barrier(grad_in), slot, 0)
        return (passed, results, act_all, coef_all)

    initial = (
        jnp.zeros((chunk, token_count, model_width), jnp.bfloat16),
        jnp.zeros((micro_count + 2 * chunk, token_count, model_width), jnp.bfloat16),
        jnp.zeros((chunk_count, expert_count * chunk * capacity, hidden), jnp.float32),
        jnp.zeros((chunk_count, expert_count * chunk * capacity, hidden), jnp.float32),
    )
    final_state = initial
    for tick_index in range(chunk_count + section_count - 1):
        final_state = tick(tick_index, final_state)
    return final_state[1][chunk : chunk + micro_count][None]


def solution(mesh):
    placed = (
        P("section", None, "expert", None),
        P("section", None, "expert", None),
        P("section", None, "expert", None),
        P("section", None, "expert"),
        P("section", None, "expert"),
        P("section", "expert", None),
        P(None, "expert", None),
    )
    return jax.shard_map(
        on_device,
        mesh=mesh,
        in_specs=placed,
        out_specs=P("section", None, "expert", None),
        check_vma=False,
    )
```
